512 devices in a mesh: grp: 16 (over z, core), shard: 32 (over x, y).
Axes of the slice: x: 4, y: 8, z: 8, core: 2. Of those that a mesh axis runs over, the one named last changes fastest.
Arguments:
- src_rows: bfloat16 [128, 128, 5376], P('grp', 'shard'), may hold values from -6 to 6
- src_act: bfloat16 [128, 128], P('grp', 'shard'), may hold values from 0.29882812 to 3
- encoder: bfloat16 [16, 32, 3, 5376, 128], P('grp', 'shard'), may hold values from -0.078125 to 0.078125
- dest_list: int32 [16, 6], replicated, may hold values from -1 to 127, as said below
- pair_list: int32 [16, 32, 18, 2], P('grp', 'shard'), may hold values from 0 to 5, as said below
- pair_count: int32 [16, 32], P('grp', 'shard'), may hold values from 1 to 18, as said below
Outputs:
- edges: bfloat16 [16, 32, 18, 128, 128], P('grp', 'shard')
The draws below stay inside these ranges and needn't reach their ends.
Inputs may be any that keep to these rules, and one draw needn't show every extreme that they name: `dest_list`: row g holds between 3 and 6 source blocks followed by -1; the blocks of one row come from distinct source groups (block // 8); some row is full. `pair_list`: entries are (slot, encoder block) with slot < 6 and block < 3; the first pair_count entries of a device are distinct pairs whose slot holds a block of its group. `pair_count`: at most 3 times the number of blocks of the device's group; some device has 18.
All inputs are finite; a program needn't handle non-finite values.
Results may differ from the reference program's by a relative error of at most 0.001.
Values may be sent and summed in bfloat16 or wider, within the bound.
No kernel may reach another device: no remote copies, remote signals or barrier semaphores. Data moves between devices by JAX's collectives and lax.ppermute only.
A program may use at most 64 MiB of HBM per device.

```python
import math
import jax
import jax.numpy as jnp
from jax import lax

D = 5376
BLK = 128
NB_G = 8
E_DEV = 3
N_SRC = 128
M = 6
P_DEV = 18
N_GRP = 16
N_SHARD = 32


def group_counts(key):
    first_key, second_key = jax.random.split(jax.random.fold_in(key, 11))
    lowest = (M + 1) // 2
    counts = jax.random.randint(first_key, (N_GRP,), lowest, M + 1)
    fullest = jax.random.randint(second_key, (), 0, N_GRP)
    rows = jnp.arange(N_GRP)
    counts = jnp.where(rows == (fullest + 1) % N_GRP, lowest, counts)
    counts = jnp.where(rows == fullest, M, counts)
    return (counts.astype(jnp.int32), fullest)


def draw_dest_list(key, part):
    counts, fullest = group_counts(key)
    source_key, local_key = jax.random.split(jax.random.fold_in(key, 21))
    orders = jax.vmap(lambda one_key: jax.random.permutation(one_key, N_GRP))(jax.random.split(source_key, N_GRP))
    rows = jnp.arange(N_GRP)[:, None]
    cols = jnp.arange(N_GRP)[None, :]
    first_entry = orders[:, :1]
    swapped = jnp.where(orders == N_GRP - 1, first_entry, jnp.where(cols == 0, N_GRP - 1, orders))
    orders = jnp.where(rows == fullest, swapped, orders)[:, :M]
    local_ids = jax.random.randint(local_key, (N_GRP, M), 0, NB_G)
    top_mark = (rows == fullest) & (jnp.arange(M)[None, :] == 0)
    local_ids = jnp.where(top_mark, NB_G - 1, local_ids)
    blocks = orders * NB_G + local_ids
    position = jnp.arange(M)[None, :]
    return jnp.where(position < counts[:, None], blocks, -1).astype(jnp.int32)


def pair_parts(key):
    counts, fullest = group_counts(key)
    order_key, first_key, second_key, pick_key = jax.random.split(jax.random.fold_in(key, 31), 4)
    total = N_GRP * N_SHARD
    orders = jax.vmap(lambda one_key: jax.random.permutation(one_key, P_DEV))(jax.random.split(order_key, total))
    orders = orders.reshape(N_GRP, N_SHARD, P_DEV)
    slot_ids = orders // E_DEV
    invalid = (slot_ids >= counts[:, None, None]).astype(jnp.int32)
    ranking = jnp.argsort(invalid, axis=-1, stable=True)
    orders = jnp.take_along_axis(orders, ranking, axis=-1)
    pairs = jnp.stack([orders // E_DEV, orders % E_DEV], axis=-1).astype(jnp.int32)
    first = jax.random.randint(first_key, (N_GRP, N_SHARD), 1, P_DEV + 1)
    second = jax.random.randint(second_key, (N_GRP, N_SHARD), 1, P_DEV + 1)
    amount = jnp.minimum(jnp.minimum(first, second), counts[:, None] * E_DEV)
    chosen = jax.random.randint(pick_key, (), 0, N_SHARD)
    is_top = (jnp.arange(N_GRP)[:, None] == fullest) & (jnp.arange(N_SHARD)[None, :] == chosen)
    amount = jnp.where(is_top, P_DEV, amount)
    return (pairs, amount.astype(jnp.int32))


def draw_pair_list(key, part):
    pairs, amount = pair_parts(key)
    return pairs


def draw_pair_count(key, part):
    pairs, amount = pair_parts(key)
    return amount


def steps_of(key, shape, cuts, least, high):
    factor_of = 1.0
    for axis_at, shards_of in cuts:
        steps = jax.random.uniform(jax.random.fold_in(jax.random.fold_in(key, 6), axis_at), (shards_of,), jnp.float32, least / len(cuts), high / len(cuts))
        factor_of = factor_of * jnp.repeat(jnp.exp(steps), shape[axis_at] // shards_of).reshape((-1,) + (1,) * (len(shape) - 1 - axis_at))
    return factor_of


def bell_draw(key, shape, deviation, bound, cuts=(), kind=jnp.bfloat16):
    result = deviation * jax.random.normal(key, shape, jnp.float32)
    if cuts:
        result = result * steps_of(key, shape, cuts, -0.22, 0.18)
    return jnp.clip(result, -bound, bound).astype(kind)


def setup_inputs(seed: int = 0) -> dict:
    keys = jax.random.split(jax.random.key(seed), 7)
    src_rows = bell_draw(keys[0], (N_SRC, BLK, D), 1.0, 6.0, ((0, 16), (1, 32)))
    src_act = jnp.clip(jnp.exp(math.log(3.0) - 2.306499 * jax.random.uniform(keys[1], (N_SRC, BLK), jnp.float32) ** steps_of(keys[1], (N_SRC, BLK), ((0, 16), (1, 32)), -0.2, 0.2)), 0.29882812, 3.0).astype(jnp.bfloat16)
    encoder = bell_draw(keys[2], (N_GRP, N_SHARD, E_DEV, D, BLK), D ** -0.5, 0.078125, ((0, 16), (1, 32)))
    dest_list = draw_dest_list(jax.random.fold_in(keys[6], 71), 0)
    pair_list = draw_pair_list(jax.random.fold_in(keys[6], 71), 0)
    pair_count = draw_pair_count(jax.random.fold_in(keys[6], 71), 0)
    return dict(src_rows=src_rows, src_act=src_act, encoder=encoder, dest_list=dest_list, pair_list=pair_list, pair_count=pair_count)


def reference(src_rows, src_act, encoder, dest_list, pair_list, pair_count):
    is_valid = dest_list >= 0
    picked = jnp.maximum(dest_list, 0).astype(jnp.int32)
    group_rows = jnp.where(is_valid[:, :, None, None], src_rows[picked], jnp.zeros((), src_rows.dtype))
    group_act = jnp.where(is_valid[:, :, None], src_act[picked], jnp.zeros((), src_act.dtype))

    def one_device(dev_index):
        group_id = dev_index // N_SHARD
        shard_id = dev_index % N_SHARD
        slot_rows = group_rows[group_id]
        slot_scale = group_act[group_id]
        weights = encoder[group_id, shard_id]
        dev_pairs = pair_list[group_id, shard_id]
        slot_ids = dev_pairs[:, 0]
        block_ids = dev_pairs[:, 1]
        left_side = slot_rows[slot_ids].astype(jnp.float32)
        right_side = weights[block_ids].astype(jnp.float32)
        tile_set = jnp.einsum("pbd,pdc->pbc", left_side, right_side)
        scaled = slot_scale[slot_ids].astype(jnp.float32)[:, :, None] * tile_set
        is_live = jnp.arange(P_DEV) < pair_count[group_id, shard_id]
        return jnp.where(is_live[:, None, None], scaled, jnp.zeros((), jnp.float32)).astype(jnp.bfloat16)

    all_edges = lax.map(one_device, jnp.arange(N_GRP * N_SHARD, dtype=jnp.int32))
    return all_edges.reshape(N_GRP, N_SHARD, P_DEV, BLK, BLK)
```

```python
import jax
import jax.numpy as jnp
from jax import lax
from jax.sharding import Mesh
from jax.sharding import PartitionSpec as P

GRP = ("z", "c")
SHARD = ("x", "y")


def local(src_rows, src_act, encoder, dest_list, pair_list, pair_count):
    n_grp = lax.psum(1, GRP)
    nb_g = src_rows.shape[0]
    width = src_rows.shape[2]
    lanes = 128
    my_group = lax.axis_index("z") * lax.psum(1, "c") + lax.axis_index("c")

    act_block = jnp.zeros(src_act.shape + (lanes,), src_rows.dtype)
    act_block = act_block.at[:, :, 0].set(src_act)
    rows_ext = jnp.concatenate([src_rows, act_block], axis=-1)

    is_valid = dest_list >= 0
    from_me = is_valid & (dest_list // nb_g == my_group)
    sel = jnp.sum(jnp.where(from_me, dest_list % nb_g, 0), axis=1)
    send = jnp.take(rows_ext, sel, axis=0)
    recv = lax.all_to_all(send, GRP, 0, 0, tiled=True)

    my_list = lax.dynamic_index_in_dim(dest_list, my_group, 0, keepdims=False)
    my_valid = my_list >= 0
    source = jnp.where(my_valid, my_list // nb_g, 0)
    slot_rows = jnp.take(recv, source, axis=0)
    slot_rows = jnp.where(my_valid[:, None, None], slot_rows, jnp.zeros((), slot_rows.dtype))

    full = lax.all_gather(slot_rows, "y", axis=1, tiled=True)
    full = lax.all_gather(full, "x", axis=1, tiled=True)

    weights = encoder[0, 0]
    weights = jnp.pad(weights, ((0, 0), (0, lanes), (0, 0)))
    dev_pairs = pair_list[0, 0]
    slot_ids = dev_pairs[:, 0]
    block_ids = dev_pairs[:, 1]
    amount = pair_count[0, 0]
    slots_total, tile_rows, ext_width = full.shape
    enc_count = weights.shape[0]
    tile_cols = weights.shape[2]
    pair_total = dev_pairs.shape[0]
    full_scale = full[:, :, width]
    stacked = full.reshape(slots_total * tile_rows, ext_width)
    products = jnp.einsum("rd,edc->rec", stacked, weights, preferred_element_type=jnp.float32)
    products = products.reshape(slots_total, tile_rows, enc_count, tile_cols)
    chosen = products[slot_ids, :, block_ids, :]
    scales = jnp.take(full_scale, slot_ids, axis=0).astype(jnp.float32)
    is_live = jnp.arange(pair_total) < amount
    result = jnp.where(
        is_live[:, None, None], scales[:, :, None] * chosen, jnp.zeros((), jnp.float32)
    ).astype(jnp.bfloat16)
    return result[None, None]


def solution(mesh):
    n_grp, n_shard = mesh.devices.shape
    n_c = 2
    n_x = 4
    devs = mesh.devices.reshape(n_grp // n_c, n_c, n_x, n_shard // n_x)
    mesh4 = Mesh(devs, ("z", "c", "x", "y"))
    return jax.shard_map(
        local,
        mesh=mesh4,
        in_specs=(
            P(GRP, SHARD, None),
            P(GRP, SHARD),
            P(GRP, SHARD, None, None, None),
            P(),
            P(GRP, SHARD, None, None),
            P(GRP, SHARD),
        ),
        out_specs=P(GRP, SHARD, None, None, None),
        check_vma=False,
    )
```

```python
import jax
import jax.numpy as jnp
from jax import lax
from jax.sharding import Mesh
from jax.sharding import PartitionSpec as P

GRP = ("z", "c")
SHARD = ("x", "y")
LANES = 128


def ring_parts(block, axis, n):
    parts = [None] * n
    parts[0] = block
    left = block
    right = block
    up = [(i, (i + 1) % n) for i in range(n)]
    down = [(i, (i - 1) % n) for i in range(n)]
    for step in range(1, n // 2 + 1):
        if 2 * step == n:
            cols = block.shape[-1]
            half = (cols // 2) // LANES * LANES
            got_left = lax.ppermute(left[..., :half], axis, up)
            got_right = lax.ppermute(right[..., half:], axis, down)
            parts[step] = jnp.concatenate([got_left, got_right], axis=-1)
        else:
            left = lax.ppermute(left, axis, up)
            right = lax.ppermute(right, axis, down)
            parts[n - step] = left
            parts[step] = right
    return parts


def local(src_rows, src_act, encoder, dest_list, pair_list, pair_count):
    nb_g = src_rows.shape[0]
    width = src_rows.shape[2]
    n_x = lax.psum(1, "x")
    n_y = lax.psum(1, "y")
    my_group = lax.axis_index("z") * lax.psum(1, "c") + lax.axis_index("c")
    my_x = lax.axis_index("x")
    my_y = lax.axis_index("y")

    act_block = jnp.zeros(src_act.shape + (LANES,), src_rows.dtype)
    act_block = act_block.at[:, :, 0].set(src_act)
    rows_ext = jnp.concatenate([src_rows, act_block], axis=-1)
    ext_width = rows_ext.shape[-1]

    is_valid = dest_list >= 0
    from_me = is_valid & (dest_list // nb_g == my_group)
    sel = jnp.sum(jnp.where(from_me, dest_list % nb_g, 0), axis=1)
    send = jnp.take(rows_ext, sel, axis=0)
    recv = lax.all_to_all(send, GRP, 0, 0, tiled=True)

    my_list = lax.dynamic_index_in_dim(dest_list, my_group, 0, keepdims=False)
    my_valid = my_list >= 0
    source = jnp.where(my_valid, my_list // nb_g, 0)
    slot_rows = jnp.take(recv, source, axis=0)
    slot_rows = jnp.where(my_valid[:, None, None], slot_rows, jnp.zeros((), slot_rows.dtype))
    slots, rows_dev, _ = slot_rows.shape

    split = (ext_width // 2) // LANES * LANES
    part_a = slot_rows[..., :split]
    part_b = slot_rows[..., split:]

    weights = encoder[0, 0]
    enc_count, _, tile_cols = weights.shape
    enc_a = weights[:, :split, :]
    enc_b = jnp.pad(weights[:, split:, :], ((0, 0), (0, ext_width - width), (0, 0)))

    def mm(block, enc):
        flat = block.reshape(-1, block.shape[-1])
        return jnp.einsum("rd,edc->rec", flat, enc, preferred_element_type=jnp.float32)

    a_x = jnp.stack(ring_parts(part_a, "x", n_x), axis=0)
    prod_a = [mm(blk, enc_a) for blk in ring_parts(a_x, "y", n_y)]
    prod_a = jnp.stack(prod_a, axis=0).reshape(n_y, n_x, slots, rows_dev, enc_count, tile_cols)

    b_y = jnp.stack(ring_parts(part_b, "y", n_y), axis=0)
    b_parts = ring_parts(b_y, "x", n_x)
    prod_b = [mm(blk, enc_b) for blk in b_parts]
    prod_b = jnp.stack(prod_b, axis=0).reshape(n_x, n_y, slots, rows_dev, enc_count, tile_cols)
    scale_b = jnp.stack([blk[..., width - split] for blk in b_parts], axis=0)

    products = prod_a + jnp.transpose(prod_b, (1, 0, 2, 3, 4, 5))

    dev_pairs = pair_list[0, 0]
    slot_ids = dev_pairs[:, 0]
    block_ids = dev_pairs[:, 1]
    amount = pair_count[0, 0]
    pair_total = dev_pairs.shape[0]

    rows_all = jnp.arange(n_x * n_y * rows_dev)
    rr = rows_all % rows_dev
    shard_abs = rows_all // rows_dev
    kx = (shard_abs // n_y - my_x) % n_x
    ky = (shard_abs % n_y - my_y) % n_y

    chosen = products[ky[None, :], kx[None, :], slot_ids[:, None], rr[None, :], block_ids[:, None], :]
    scales = scale_b[kx[None, :], ky[None, :], slot_ids[:, None], rr[None, :]].astype(jnp.float32)
    is_live = jnp.arange(pair_total) < amount
    result = jnp.where(
        is_live[:, None, None], scales[:, :, None] * chosen, jnp.zeros((), jnp.float32)
    ).astype(jnp.bfloat16)
    return result[None, None]


def solution(mesh):
    n_grp, n_shard = mesh.devices.shape
    n_c = 2
    n_x = 4
    devs = mesh.devices.reshape(n_grp // n_c, n_c, n_x, n_shard // n_x)
    mesh4 = Mesh(devs, ("z", "c", "x", "y"))
    return jax.shard_map(
        local,
        mesh=mesh4,
        in_specs=(
            P(GRP, SHARD, None),
            P(GRP, SHARD),
            P(GRP, SHARD, None, None, None),
            P(),
            P(GRP, SHARD, None, None),
            P(GRP, SHARD),
        ),
        out_specs=P(GRP, SHARD, None, None, None),
        check_vma=False,
    )
```

```python
import jax
import jax.numpy as jnp
from jax import lax
from jax.sharding import Mesh
from jax.sharding import PartitionSpec as P

GRP = ("z", "c")
SHARD = ("x", "y")
LANES = 128


def ring_parts(block, axis, n):
    parts = [None] * n
    parts[0] = block
    left = block
    right = block
    up = [(i, (i + 1) % n) for i in range(n)]
    down = [(i, (i - 1) % n) for i in range(n)]
    for step in range(1, n // 2 + 1):
        if 2 * step == n:
            cols = block.shape[-1]
            half = (cols // 2) // LANES * LANES
            got_left = lax.ppermute(left[..., :half], axis, up)
            got_right = lax.ppermute(right[..., half:], axis, down)
            parts[step] = jnp.concatenate([got_left, got_right], axis=-1)
        else:
            left = lax.ppermute(left, axis, up)
            right = lax.ppermute(right, axis, down)
            parts[n - step] = left
            parts[step] = right
    return parts


def local(src_rows, src_act, encoder, dest_list, pair_list, pair_count):
    nb_g = src_rows.shape[0]
    width = src_rows.shape[2]
    n_x = lax.psum(1, "x")
    n_y = lax.psum(1, "y")
    my_group = lax.axis_index("z") * lax.psum(1, "c") + lax.axis_index("c")
    my_x = lax.axis_index("x")
    my_y = lax.axis_index("y")

    act_block = jnp.zeros(src_act.shape + (LANES,), src_rows.dtype)
    act_block = act_block.at[:, :, 0].set(src_act)
    rows_ext = jnp.concatenate([src_rows, act_block], axis=-1)
    ext_width = rows_ext.shape[-1]

    is_valid = dest_list >= 0
    from_me = is_valid & (dest_list // nb_g == my_group)
    sel = jnp.sum(jnp.where(from_me, dest_list % nb_g, 0), axis=1)
    send = jnp.take(rows_ext, sel, axis=0)
    recv = lax.all_to_all(send, GRP, 0, 0, tiled=True)

    my_list = lax.dynamic_index_in_dim(dest_list, my_group, 0, keepdims=False)
    my_valid = my_list >= 0
    source = jnp.where(my_valid, my_list // nb_g, 0)
    slot_rows = jnp.take(recv, source, axis=0)
    slot_rows = jnp.where(my_valid[:, None, None], slot_rows, jnp.zeros((), slot_rows.dtype))
    slots, rows_dev, _ = slot_rows.shape

    split = (ext_width // 2) // LANES * LANES
    part_a = slot_rows[..., :split]
    part_b = slot_rows[..., split:]

    weights = encoder[0, 0]
    enc_count, _, tile_cols = weights.shape
    enc_a = weights[:, :split, :]
    enc_b = jnp.pad(weights[:, split:, :], ((0, 0), (0, ext_width - width), (0, 0)))

    def mm(block, enc):
        flat = block.reshape(-1, block.shape[-1])
        return jnp.einsum("rd,edc->rec", flat, enc, preferred_element_type=jnp.float32)

    a_x = lax.all_gather(part_a, "x", axis=0, tiled=False)
    a_all = lax.all_gather(a_x, "y", axis=1, tiled=False)
    prod_a = mm(a_all, enc_a).reshape(n_x, n_y, slots, rows_dev, enc_count, tile_cols)

    b_y = jnp.stack(ring_parts(part_b, "y", n_y), axis=0)
    b_parts = ring_parts(b_y, "x", n_x)
    prod_b = jnp.stack([mm(blk, enc_b) for blk in b_parts], axis=0)
    prod_b = prod_b.reshape(n_x, n_y, slots, rows_dev, enc_count, tile_cols)
    prod_b = jnp.roll(jnp.roll(prod_b, my_x, axis=0), my_y, axis=1)
    scale_b = jnp.stack([blk[..., width - split] for blk in b_parts], axis=0)
    scale_b = jnp.roll(jnp.roll(scale_b, my_x, axis=0), my_y, axis=1)

    products = prod_a + prod_b
    tiles = jnp.transpose(products, (2, 4, 0, 1, 3, 5)).reshape(slots * enc_count, -1, tile_cols)
    scale_rows = jnp.transpose(scale_b, (2, 0, 1, 3)).reshape(slots, -1)

    dev_pairs = pair_list[0, 0]
    slot_ids = dev_pairs[:, 0]
    block_ids = dev_pairs[:, 1]
    amount = pair_count[0, 0]
    pair_total = dev_pairs.shape[0]
    chosen = jnp.take(tiles, slot_ids * enc_count + block_ids, axis=0)
    scales = jnp.take(scale_rows, slot_ids, axis=0).astype(jnp.float32)
    is_live = jnp.arange(pair_total) < amount
    result = jnp.where(
        is_live[:, None, None], scales[:, :, None] * chosen, jnp.zeros((), jnp.float32)
    ).astype(jnp.bfloat16)
    return result[None, None]


def solution(mesh):
    n_grp, n_shard = mesh.devices.shape
    n_c = 2
    n_x = 4
    devs = mesh.devices.reshape(n_grp // n_c, n_c, n_x, n_shard // n_x)
    mesh4 = Mesh(devs, ("z", "c", "x", "y"))
    return jax.shard_map(
        local,
        mesh=mesh4,
        in_specs=(
            P(GRP, SHARD, None),
            P(GRP, SHARD),
            P(GRP, SHARD, None, None, None),
            P(),
            P(GRP, SHARD, None, None),
            P(GRP, SHARD),
        ),
        out_specs=P(GRP, SHARD, None, None, None),
        check_vma=False,
    )
```

```python
import jax
import jax.numpy as jnp
from jax import lax
from jax.sharding import Mesh
from jax.sharding import PartitionSpec as P

GRP = ("z", "c")
SHARD = ("x", "y")
LANES = 128


def ring_parts(block, axis, n):
    parts = [None] * n
    parts[0] = block
    left = block
    right = block
    up = [(i, (i + 1) % n) for i in range(n)]
    down = [(i, (i - 1) % n) for i in range(n)]
    for step in range(1, n // 2 + 1):
        if 2 * step == n:
            cols = block.shape[-1]
            half = (cols // 2) // LANES * LANES
            got_left = lax.ppermute(left[..., :half], axis, up)
            got_right = lax.ppermute(right[..., half:], axis, down)
            parts[step] = jnp.concatenate([got_left, got_right], axis=-1)
        else:
            left = lax.ppermute(left, axis, up)
            right = lax.ppermute(right, axis, down)
            parts[n - step] = left
            parts[step] = right
    return parts


def local(src_rows, src_act, encoder, dest_list, pair_list, pair_count):
    nb_g = src_rows.shape[0]
    width = src_rows.shape[2]
    n_x = lax.psum(1, "x")
    n_y = lax.psum(1, "y")
    my_group = lax.axis_index("z") * lax.psum(1, "c") + lax.axis_index("c")
    my_x = lax.axis_index("x")
    my_y = lax.axis_index("y")

    act_block = jnp.zeros(src_act.shape + (LANES,), src_rows.dtype)
    act_block = act_block.at[:, :, 0].set(src_act)
    rows_ext = jnp.concatenate([src_rows, act_block], axis=-1)
    ext_width = rows_ext.shape[-1]

    is_valid = dest_list >= 0
    from_me = is_valid & (dest_list // nb_g == my_group)
    sel = jnp.sum(jnp.where(from_me, dest_list % nb_g, 0), axis=1)
    send = jnp.take(rows_ext, sel, axis=0)
    recv = lax.all_to_all(send, GRP, 0, 0, tiled=True)

    my_list = lax.dynamic_index_in_dim(dest_list, my_group, 0, keepdims=False)
    my_valid = my_list >= 0
    source = jnp.where(my_valid, my_list // nb_g, 0)
    slot_rows = jnp.take(recv, source, axis=0)
    slot_rows = jnp.where(my_valid[:, None, None], slot_rows, jnp.zeros((), slot_rows.dtype))
    slots, rows_dev, _ = slot_rows.shape

    split = (ext_width * 3 // 5) // LANES * LANES
    part_a = slot_rows[..., :split]
    part_b = slot_rows[..., split:]

    weights = encoder[0, 0]
    enc_count, _, tile_cols = weights.shape
    enc_a = weights[:, :split, :]
    enc_b = jnp.pad(weights[:, split:, :], ((0, 0), (0, ext_width - width), (0, 0)))

    def mm(block, enc):
        flat = block.reshape(-1, block.shape[-1])
        return jnp.einsum("rd,edc->rec", flat, enc, preferred_element_type=jnp.float32)

    a_all = lax.all_gather(part_a, SHARD, axis=0, tiled=False)
    prod_a = mm(a_all, enc_a).reshape(n_x, n_y, slots, rows_dev, enc_count, tile_cols)

    b_y = jnp.stack(ring_parts(part_b, "y", n_y), axis=0)
    b_parts = ring_parts(b_y, "x", n_x)
    prod_b = jnp.stack([mm(blk, enc_b) for blk in b_parts], axis=0)
    prod_b = prod_b.reshape(n_x, n_y, slots, rows_dev, enc_count, tile_cols)
    prod_b = jnp.roll(jnp.roll(prod_b, my_x, axis=0), my_y, axis=1)
    scale_b = jnp.stack([blk[..., width - split] for blk in b_parts], axis=0)
    scale_b = jnp.roll(jnp.roll(scale_b, my_x, axis=0), my_y, axis=1)

    products = prod_a + prod_b
    tiles = jnp.transpose(products, (2, 4, 0, 1, 3, 5)).reshape(slots * enc_count, -1, tile_cols)
    scale_rows = jnp.transpose(scale_b, (2, 0, 1, 3)).reshape(slots, -1)

    dev_pairs = pair_list[0, 0]
    slot_ids = dev_pairs[:, 0]
    block_ids = dev_pairs[:, 1]
    amount = pair_count[0, 0]
    pair_total = dev_pairs.shape[0]
    chosen = jnp.take(tiles, slot_ids * enc_count + block_ids, axis=0)
    scales = jnp.take(scale_rows, slot_ids, axis=0).astype(jnp.float32)
    is_live = jnp.arange(pair_total) < amount
    result = jnp.where(
        is_live[:, None, None], scales[:, :, None] * chosen, jnp.zeros((), jnp.float32)
    ).astype(jnp.bfloat16)
    return result[None, None]


def solution(mesh):
    n_grp, n_shard = mesh.devices.shape
    n_c = 2
    n_x = 4
    devs = mesh.devices.reshape(n_grp // n_c, n_c, n_x, n_shard // n_x)
    mesh4 = Mesh(devs, ("z", "c", "x", "y"))
    return jax.shard_map(
        local,
        mesh=mesh4,
        in_specs=(
            P(GRP, SHARD, None),
            P(GRP, SHARD),
            P(GRP, SHARD, None, None, None),
            P(),
            P(GRP, SHARD, None, None),
            P(GRP, SHARD),
        ),
        out_specs=P(GRP, SHARD, None, None, None),
        check_vma=False,
    )
```

```python
import jax
import jax.numpy as jnp
from jax import lax
from jax.sharding import Mesh
from jax.sharding import PartitionSpec as P

GRP = ("z", "c")
SHARD = ("x", "y")
LANES = 128


def ring_parts(block, axis, n):
    parts = [None] * n
    parts[0] = block
    left = block
    right = block
    up = [(i, (i + 1) % n) for i in range(n)]
    down = [(i, (i - 1) % n) for i in range(n)]
    for step in range(1, n // 2 + 1):
        if 2 * step == n:
            half = block.shape[0] // 2
            got_left = lax.ppermute(left[:half], axis, up)
            got_right = lax.ppermute(right[half:], axis, down)
            parts[step] = jnp.concatenate([got_left, got_right], axis=0)
        else:
            left = lax.ppermute(left, axis, up)
            right = lax.ppermute(right, axis, down)
            parts[n - step] = left
            parts[step] = right
    return parts


def local(src_rows, src_act, encoder, dest_list, pair_list, pair_count):
    nb_g = src_rows.shape[0]
    width = src_rows.shape[2]
    n_x = lax.psum(1, "x")
    n_y = lax.psum(1, "y")
    my_group = lax.axis_index("z") * lax.psum(1, "c") + lax.axis_index("c")
    my_x = lax.axis_index("x")
    my_y = lax.axis_index("y")

    act_block = jnp.zeros(src_act.shape + (LANES,), src_rows.dtype)
    act_block = act_block.at[:, :, 0].set(src_act)
    rows_ext = jnp.concatenate([src_rows, act_block], axis=-1)
    ext_width = rows_ext.shape[-1]

    is_valid = dest_list >= 0
    from_me = is_valid & (dest_list // nb_g == my_group)
    sel = jnp.sum(jnp.where(from_me, dest_list % nb_g, 0), axis=1)
    send = jnp.take(rows_ext, sel, axis=0)
    recv = lax.all_to_all(send, GRP, 0, 0, tiled=True)

    my_list = lax.dynamic_index_in_dim(dest_list, my_group, 0, keepdims=False)
    my_valid = my_list >= 0
    source = jnp.where(my_valid, my_list // nb_g, 0)
    slot_rows = jnp.take(recv, source, axis=0)
    slot_rows = jnp.where(my_valid[:, None, None], slot_rows, jnp.zeros((), slot_rows.dtype))
    slots, rows_dev, _ = slot_rows.shape

    split = (ext_width * 3 // 5) // LANES * LANES
    part_a = slot_rows[..., :split]
    part_b = slot_rows[..., split:]

    weights = encoder[0, 0]
    enc_count, _, tile_cols = weights.shape
    enc_a = weights[:, :split, :]
    enc_b = jnp.pad(weights[:, split:, :], ((0, 0), (0, ext_width - width), (0, 0)))

    def mm(block, enc):
        flat = block.reshape(-1, block.shape[-1])
        return jnp.einsum("rd,edc->rec", flat, enc, preferred_element_type=jnp.float32)

    a_all = lax.all_gather(part_a, SHARD, axis=0, tiled=False)
    prod_a = mm(a_all, enc_a).reshape(n_x, n_y, slots, rows_dev, enc_count, tile_cols)

    b_y = jnp.stack(ring_parts(part_b, "y", n_y), axis=0)
    b_parts = ring_parts(b_y, "x", n_x)
    prod_b = jnp.stack([mm(blk, enc_b) for blk in b_parts], axis=0)
    prod_b = prod_b.reshape(n_x, n_y, slots, rows_dev, enc_count, tile_cols)
    prod_b = jnp.roll(jnp.roll(prod_b, my_x, axis=0), my_y, axis=1)
    scale_b = jnp.stack([blk[..., width - split] for blk in b_parts], axis=0)
    scale_b = jnp.roll(jnp.roll(scale_b, my_x, axis=0), my_y, axis=1)

    products = prod_a + prod_b
    tiles = jnp.transpose(products, (2, 4, 0, 1, 3, 5)).reshape(slots * enc_count, -1, tile_cols)
    scale_rows = jnp.transpose(scale_b, (2, 0, 1, 3)).reshape(slots, -1)

    dev_pairs = pair_list[0, 0]
    slot_ids = dev_pairs[:, 0]
    block_ids = dev_pairs[:, 1]
    amount = pair_count[0, 0]
    pair_total = dev_pairs.shape[0]
    chosen = jnp.take(tiles, slot_ids * enc_count + block_ids, axis=0)
    scales = jnp.take(scale_rows, slot_ids, axis=0).astype(jnp.float32)
    is_live = jnp.arange(pair_total) < amount
    result = jnp.where(
        is_live[:, None, None], scales[:, :, None] * chosen, jnp.zeros((), jnp.float32)
    ).astype(jnp.bfloat16)
    return result[None, None]


def solution(mesh):
    n_grp, n_shard = mesh.devices.shape
    n_c = 2
    n_x = 4
    devs = mesh.devices.reshape(n_grp // n_c, n_c, n_x, n_shard // n_x)
    mesh4 = Mesh(devs, ("z", "c", "x", "y"))
    return jax.shard_map(
        local,
        mesh=mesh4,
        in_specs=(
            P(GRP, SHARD, None),
            P(GRP, SHARD),
            P(GRP, SHARD, None, None, None),
            P(),
            P(GRP, SHARD, None, None),
            P(GRP, SHARD),
        ),
        out_specs=P(GRP, SHARD, None, None, None),
        check_vma=False,
    )
```

```python
import jax
import jax.numpy as jnp
from jax import lax
from jax.sharding import Mesh
from jax.sharding import PartitionSpec as P

GRP = ("z", "c")
SHARD = ("x", "y")
LANES = 128


def ring_parts(block, axis, n):
    parts = [None] * n
    parts[0] = block
    left = block
    right = block
    up = [(i, (i + 1) % n) for i in range(n)]
    down = [(i, (i - 1) % n) for i in range(n)]
    for step in range(1, n // 2 + 1):
        if 2 * step == n:
            half = block.shape[0] // 2
            got_left = lax.ppermute(left[:half], axis, up)
            got_right = lax.ppermute(right[half:], axis, down)
            parts[step] = jnp.concatenate([got_left, got_right], axis=0)
        else:
            left = lax.ppermute(left, axis, up)
            right = lax.ppermute(right, axis, down)
            parts[n - step] = left
            parts[step] = right
    return parts


def local(src_rows, src_act, encoder, dest_list, pair_list, pair_count):
    nb_g = src_rows.shape[0]
    width = src_rows.shape[2]
    n_x = lax.psum(1, "x")
    n_y = lax.psum(1, "y")
    my_group = lax.axis_index("z") * lax.psum(1, "c") + lax.axis_index("c")
    my_x = lax.axis_index("x")
    my_y = lax.axis_index("y")

    act_block = jnp.zeros(src_act.shape + (LANES,), src_rows.dtype)
    act_block = act_block.at[:, :, 0].set(src_act)
    rows_ext = jnp.concatenate([src_rows, act_block], axis=-1)
    ext_width = rows_ext.shape[-1]

    is_valid = dest_list >= 0
    from_me = is_valid & (dest_list // nb_g == my_group)
    sel = jnp.sum(jnp.where(from_me, dest_list % nb_g, 0), axis=1)
    send = jnp.take(rows_ext, sel, axis=0)
    recv = lax.all_to_all(send, GRP, 0, 0, tiled=True)

    my_list = lax.dynamic_index_in_dim(dest_list, my_group, 0, keepdims=False)
    my_valid = my_list >= 0
    source = jnp.where(my_valid, my_list // nb_g, 0)
    slot_rows = jnp.take(recv, source, axis=0)
    slot_rows = jnp.where(my_valid[:, None, None], slot_rows, jnp.zeros((), slot_rows.dtype))
    slots, rows_dev, _ = slot_rows.shape

    split = (ext_width * 5 // 9 + LANES - 1) // LANES * LANES
    part_a = slot_rows[..., :split]
    part_b = slot_rows[..., split:]

    weights = encoder[0, 0]
    enc_count, _, tile_cols = weights.shape
    enc_a = weights[:, :split, :]
    enc_b = jnp.pad(weights[:, split:, :], ((0, 0), (0, ext_width - width), (0, 0)))

    def mm(block, enc):
        flat = block.reshape(-1, block.shape[-1])
        return jnp.einsum("rd,edc->rec", flat, enc, preferred_element_type=jnp.float32)

    a_all = lax.all_gather(part_a, SHARD, axis=0, tiled=False)
    prod_a = mm(a_all, enc_a).reshape(n_x, n_y, slots, rows_dev, enc_count, tile_cols)

    b_y = jnp.stack(ring_parts(part_b, "y", n_y), axis=0)
    b_parts = ring_parts(b_y, "x", n_x)
    prod_b = jnp.stack([mm(blk, enc_b) for blk in b_parts], axis=0)
    prod_b = prod_b.reshape(n_x, n_y, slots, rows_dev, enc_count, tile_cols)
    prod_b = jnp.roll(jnp.roll(prod_b, my_x, axis=0), my_y, axis=1)
    scale_b = jnp.stack([blk[..., width - split] for blk in b_parts], axis=0)
    scale_b = jnp.roll(jnp.roll(scale_b, my_x, axis=0), my_y, axis=1)

    products = prod_a + prod_b
    tiles = jnp.transpose(products, (2, 4, 0, 1, 3, 5)).reshape(slots * enc_count, -1, tile_cols)
    scale_rows = jnp.transpose(scale_b, (2, 0, 1, 3)).reshape(slots, -1)

    dev_pairs = pair_list[0, 0]
    slot_ids = dev_pairs[:, 0]
    block_ids = dev_pairs[:, 1]
    amount = pair_count[0, 0]
    pair_total = dev_pairs.shape[0]
    chosen = jnp.take(tiles, slot_ids * enc_count + block_ids, axis=0)
    scales = jnp.take(scale_rows, slot_ids, axis=0).astype(jnp.float32)
    is_live = jnp.arange(pair_total) < amount
    result = jnp.where(
        is_live[:, None, None], scales[:, :, None] * chosen, jnp.zeros((), jnp.float32)
    ).astype(jnp.bfloat16)
    return result[None, None]


def solution(mesh):
    n_grp, n_shard = mesh.devices.shape
    n_c = 2
    n_x = 4
    devs = mesh.devices.reshape(n_grp // n_c, n_c, n_x, n_shard // n_x)
    mesh4 = Mesh(devs, ("z", "c", "x", "y"))
    return jax.shard_map(
        local,
        mesh=mesh4,
        in_specs=(
            P(GRP, SHARD, None),
            P(GRP, SHARD),
            P(GRP, SHARD, None, None, None),
            P(),
            P(GRP, SHARD, None, None),
            P(GRP, SHARD),
        ),
        out_specs=P(GRP, SHARD, None, None, None),
        check_vma=False,
    )
```

```python
import jax
import jax.numpy as jnp
from jax import lax
from jax.sharding import Mesh
from jax.sharding import PartitionSpec as P

GRP = ("z", "c")
SHARD = ("x", "y")
LANES = 128


def ring_parts(block, axis, n):
    parts = [None] * n
    parts[0] = block
    left = block
    right = block
    up = [(i, (i + 1) % n) for i in range(n)]
    down = [(i, (i - 1) % n) for i in range(n)]
    for step in range(1, n // 2 + 1):
        if 2 * step == n:
            half = block.shape[0] // 2
            got_left = lax.ppermute(left[:half], axis, up)
            got_right = lax.ppermute(right[half:], axis, down)
            parts[step] = jnp.concatenate([got_left, got_right], axis=0)
        else:
            left = lax.ppermute(left, axis, up)
            right = lax.ppermute(right, axis, down)
            parts[n - step] = left
            parts[step] = right
    return parts


def local(src_rows, src_act, encoder, dest_list, pair_list, pair_count):
    nb_g = src_rows.shape[0]
    width = src_rows.shape[2]
    n_x = lax.psum(1, "x")
    n_y = lax.psum(1, "y")
    my_group = lax.axis_index("z") * lax.psum(1, "c") + lax.axis_index("c")
    my_x = lax.axis_index("x")
    my_y = lax.axis_index("y")

    act_block = jnp.zeros(src_act.shape + (LANES,), src_rows.dtype)
    act_block = act_block.at[:, :, 0].set(src_act)
    rows_ext = jnp.concatenate([src_rows, act_block], axis=-1)
    ext_width = rows_ext.shape[-1]

    is_valid = dest_list >= 0
    from_me = is_valid & (dest_list // nb_g == my_group)
    sel = jnp.sum(jnp.where(from_me, dest_list % nb_g, 0), axis=1)
    send = jnp.take(rows_ext, sel, axis=0)
    recv = lax.all_to_all(send, GRP, 0, 0, tiled=True)

    my_list = lax.dynamic_index_in_dim(dest_list, my_group, 0, keepdims=False)
    my_valid = my_list >= 0
    source = jnp.where(my_valid, my_list // nb_g, 0)
    slot_rows = jnp.take(recv, source, axis=0)
    slot_rows = jnp.where(my_valid[:, None, None], slot_rows, jnp.zeros((), slot_rows.dtype))
    slots, rows_dev, _ = slot_rows.shape

    split = (ext_width * 3 // 5) // LANES * LANES
    part_a = slot_rows[..., :split]
    part_b = slot_rows[..., split:]

    weights = encoder[0, 0]
    enc_count, _, tile_cols = weights.shape
    enc_a = weights[:, :split, :]
    enc_b = jnp.pad(weights[:, split:, :], ((0, 0), (0, ext_width - width), (0, 0)))

    def mm(block, enc):
        flat = block.reshape(-1, block.shape[-1])
        return jnp.einsum("rd,edc->rec", flat, enc, preferred_element_type=jnp.float32)

    flat_a = part_a.reshape(slots * rows_dev, split)
    a_all = lax.all_gather(flat_a, SHARD, axis=0, tiled=False)
    prod_a = mm(a_all, enc_a).reshape(n_x, n_y, slots, rows_dev, enc_count, tile_cols)

    b_y = jnp.stack(ring_parts(part_b, "y", n_y), axis=0)
    b_parts = ring_parts(b_y, "x", n_x)
    prod_b = jnp.stack([mm(blk, enc_b) for blk in b_parts], axis=0)
    prod_b = prod_b.reshape(n_x, n_y, slots, rows_dev, enc_count, tile_cols)
    prod_b = jnp.roll(jnp.roll(prod_b, my_x, axis=0), my_y, axis=1)
    scale_b = jnp.stack([blk[..., width - split] for blk in b_parts], axis=0)
    scale_b = jnp.roll(jnp.roll(scale_b, my_x, axis=0), my_y, axis=1)

    products = prod_a + prod_b
    tiles = jnp.transpose(products, (2, 4, 0, 1, 3, 5)).reshape(slots * enc_count, -1, tile_cols)
    scale_rows = jnp.transpose(scale_b, (2, 0, 1, 3)).reshape(slots, -1)

    dev_pairs = pair_list[0, 0]
    slot_ids = dev_pairs[:, 0]
    block_ids = dev_pairs[:, 1]
    amount = pair_count[0, 0]
    pair_total = dev_pairs.shape[0]
    chosen = jnp.take(tiles, slot_ids * enc_count + block_ids, axis=0)
    scales = jnp.take(scale_rows, slot_ids, axis=0).astype(jnp.float32)
    is_live = jnp.arange(pair_total) < amount
    result = jnp.where(
        is_live[:, None, None], scales[:, :, None] * chosen, jnp.zeros((), jnp.float32)
    ).astype(jnp.bfloat16)
    return result[None, None]


def solution(mesh):
    n_grp, n_shard = mesh.devices.shape
    n_c = 2
    n_x = 4
    devs = mesh.devices.reshape(n_grp // n_c, n_c, n_x, n_shard // n_x)
    mesh4 = Mesh(devs, ("z", "c", "x", "y"))
    return jax.shard_map(
        local,
        mesh=mesh4,
        in_specs=(
            P(GRP, SHARD, None),
            P(GRP, SHARD),
            P(GRP, SHARD, None, None, None),
            P(),
            P(GRP, SHARD, None, None),
            P(GRP, SHARD),
        ),
        out_specs=P(GRP, SHARD, None, None, None),
        check_vma=False,
    )
```

```python
import jax
import jax.numpy as jnp
from jax import lax
from jax.sharding import Mesh
from jax.sharding import PartitionSpec as P

GRP = ("z", "c")
SHARD = ("x", "y")
LANES = 128


def ring_parts(block, axis, n):
    parts = [None] * n
    parts[0] = block
    left = block
    right = block
    up = [(i, (i + 1) % n) for i in range(n)]
    down = [(i, (i - 1) % n) for i in range(n)]
    for step in range(1, n // 2 + 1):
        if 2 * step == n:
            half = block.shape[0] // 2
            got_left = lax.ppermute(left[:half], axis, up)
            got_right = lax.ppermute(right[half:], axis, down)
            parts[step] = jnp.concatenate([got_left, got_right], axis=0)
        else:
            left = lax.ppermute(left, axis, up)
            right = lax.ppermute(right, axis, down)
            parts[n - step] = left
            parts[step] = right
    return parts


def local(src_rows, src_act, encoder, dest_list, pair_list, pair_count):
    nb_g = src_rows.shape[0]
    width = src_rows.shape[2]
    n_x = lax.psum(1, "x")
    n_y = lax.psum(1, "y")
    my_group = lax.axis_index("z") * lax.psum(1, "c") + lax.axis_index("c")
    my_x = lax.axis_index("x")
    my_y = lax.axis_index("y")

    ext_width = width + LANES

    is_valid = dest_list >= 0
    from_me = is_valid & (dest_list // nb_g == my_group)
    sel = jnp.sum(jnp.where(from_me, dest_list % nb_g, 0), axis=1)
    send_act = jnp.take(src_act, sel, axis=0, mode="clip")
    act_block = jnp.zeros(send_act.shape + (LANES,), src_rows.dtype)
    act_block = act_block.at[:, :, 0].set(send_act)
    send = jnp.concatenate([jnp.take(src_rows, sel, axis=0, mode="clip"), act_block], axis=-1)
    recv = lax.all_to_all(send, GRP, 0, 0, tiled=True)

    my_list = lax.dynamic_index_in_dim(dest_list, my_group, 0, keepdims=False)
    my_valid = my_list >= 0
    source = jnp.where(my_valid, my_list // nb_g, 0)
    slot_rows = jnp.take(recv, source, axis=0, mode="clip")
    slot_rows = jnp.where(my_valid[:, None, None], slot_rows, jnp.zeros((), slot_rows.dtype))
    slots, rows_dev, _ = slot_rows.shape

    split = (ext_width * 3 // 5) // LANES * LANES
    part_a = slot_rows[..., :split]
    part_b = slot_rows[..., split:]

    weights = encoder[0, 0]
    enc_count, _, tile_cols = weights.shape
    enc_a = weights[:, :split, :]
    enc_b = jnp.pad(weights[:, split:, :], ((0, 0), (0, ext_width - width), (0, 0)))

    def mm(block, enc):
        flat = block.reshape(-1, block.shape[-1])
        return jnp.einsum("rd,edc->rec", flat, enc, preferred_element_type=jnp.float32)

    a_all = lax.all_gather(part_a, SHARD, axis=0, tiled=False)
    prod_a = mm(a_all, enc_a).reshape(n_x, n_y, slots, rows_dev, enc_count, tile_cols)

    b_y = jnp.stack(ring_parts(part_b, "y", n_y), axis=0)
    b_parts = ring_parts(b_y, "x", n_x)
    prod_b = jnp.stack([mm(blk, enc_b) for blk in b_parts], axis=0)
    prod_b = prod_b.reshape(n_x, n_y, slots, rows_dev, enc_count, tile_cols)
    prod_b = jnp.roll(jnp.roll(prod_b, my_x, axis=0), my_y, axis=1)
    scale_b = jnp.stack([blk[..., width - split] for blk in b_parts], axis=0)
    scale_b = jnp.roll(jnp.roll(scale_b, my_x, axis=0), my_y, axis=1)

    products = prod_a + prod_b
    tiles = jnp.transpose(products, (2, 4, 0, 1, 3, 5)).reshape(slots * enc_count, -1, tile_cols)
    scale_rows = jnp.transpose(scale_b, (2, 0, 1, 3)).reshape(slots, -1)

    dev_pairs = pair_list[0, 0]
    slot_ids = dev_pairs[:, 0]
    block_ids = dev_pairs[:, 1]
    amount = pair_count[0, 0]
    pair_total = dev_pairs.shape[0]
    chosen = jnp.take(tiles, slot_ids * enc_count + block_ids, axis=0, mode="clip")
    scales = jnp.take(scale_rows, slot_ids, axis=0, mode="clip").astype(jnp.float32)
    is_live = jnp.arange(pair_total) < amount
    result = jnp.where(
        is_live[:, None, None], scales[:, :, None] * chosen, jnp.zeros((), jnp.float32)
    ).astype(jnp.bfloat16)
    return result[None, None]


def solution(mesh):
    n_grp, n_shard = mesh.devices.shape
    n_c = 2
    n_x = 4
    devs = mesh.devices.reshape(n_grp // n_c, n_c, n_x, n_shard // n_x)
    mesh4 = Mesh(devs, ("z", "c", "x", "y"))
    return jax.shard_map(
        local,
        mesh=mesh4,
        in_specs=(
            P(GRP, SHARD, None),
            P(GRP, SHARD),
            P(GRP, SHARD, None, None, None),
            P(),
            P(GRP, SHARD, None, None),
            P(GRP, SHARD),
        ),
        out_specs=P(GRP, SHARD, None, None, None),
        check_vma=False,
    )
```

```python
import jax
import jax.numpy as jnp
from jax import lax
from jax.sharding import Mesh
from jax.sharding import PartitionSpec as P

GRP = ("z", "c")
SHARD = ("x", "y")
LANES = 128


def ring_parts(block, axis, n):
    parts = [None] * n
    parts[0] = block
    left = block
    right = block
    up = [(i, (i + 1) % n) for i in range(n)]
    down = [(i, (i - 1) % n) for i in range(n)]
    for step in range(1, n // 2 + 1):
        if 2 * step == n:
            half = block.shape[0] // 2
            got_left = lax.ppermute(left[:half], axis, up)
            got_right = lax.ppermute(right[half:], axis, down)
            parts[step] = jnp.concatenate([got_left, got_right], axis=0)
        else:
            left = lax.ppermute(left, axis, up)
            right = lax.ppermute(right, axis, down)
            parts[n - step] = left
            parts[step] = right
    return parts


def local(src_rows, src_act, encoder, dest_list, pair_list, pair_count):
    nb_g = src_rows.shape[0]
    width = src_rows.shape[2]
    n_x = lax.psum(1, "x")
    n_y = lax.psum(1, "y")
    my_group = lax.axis_index("z") * lax.psum(1, "c") + lax.axis_index("c")
    my_x = lax.axis_index("x")
    my_y = lax.axis_index("y")

    ext_width = width + LANES

    is_valid = dest_list >= 0
    from_me = is_valid & (dest_list // nb_g == my_group)
    sel = jnp.sum(jnp.where(from_me, dest_list % nb_g, 0), axis=1)
    send_act = jnp.take(src_act, sel, axis=0, mode="clip")
    act_block = jnp.zeros(send_act.shape + (LANES,), src_rows.dtype)
    act_block = act_block.at[:, :, 0].set(send_act)
    send = jnp.concatenate([jnp.take(src_rows, sel, axis=0, mode="clip"), act_block], axis=-1)
    recv = lax.all_to_all(send, GRP, 0, 0, tiled=True)

    my_list = lax.dynamic_index_in_dim(dest_list, my_group, 0, keepdims=False)
    my_valid = my_list >= 0
    source = jnp.where(my_valid, my_list // nb_g, 0)
    slot_rows = jnp.take(recv, source, axis=0, mode="clip")
    slot_rows = jnp.where(my_valid[:, None, None], slot_rows, jnp.zeros((), slot_rows.dtype))
    slots, rows_dev, _ = slot_rows.shape

    split = (ext_width * 3 // 5) // LANES * LANES
    part_a = slot_rows[..., :split]
    part_b = slot_rows[..., split:]

    weights = encoder[0, 0]
    enc_count, _, tile_cols = weights.shape
    enc_a = jnp.transpose(weights[:, :split, :], (1, 0, 2)).reshape(split, enc_count * tile_cols)
    enc_b = jnp.pad(weights[:, split:, :], ((0, 0), (0, ext_width - width), (0, 0)))
    enc_b = jnp.transpose(enc_b, (1, 0, 2)).reshape(ext_width - split, enc_count * tile_cols)

    def mm(block, enc):
        flat = block.reshape(-1, block.shape[-1])
        out = jnp.dot(flat, enc, preferred_element_type=jnp.float32)
        return out.reshape(-1, enc_count, tile_cols)

    a_all = lax.all_gather(part_a, SHARD, axis=0, tiled=False)
    prod_a = mm(a_all, enc_a).reshape(n_x, n_y, slots, rows_dev, enc_count, tile_cols)

    b_y = jnp.stack(ring_parts(part_b, "y", n_y), axis=0)
    b_parts = ring_parts(b_y, "x", n_x)
    prod_b = jnp.stack([mm(blk, enc_b) for blk in b_parts], axis=0)
    prod_b = prod_b.reshape(n_x, n_y, slots, rows_dev, enc_count, tile_cols)
    prod_b = jnp.roll(jnp.roll(prod_b, my_x, axis=0), my_y, axis=1)
    scale_b = jnp.stack([blk[..., width - split] for blk in b_parts], axis=0)
    scale_b = jnp.roll(jnp.roll(scale_b, my_x, axis=0), my_y, axis=1)

    products = prod_a + prod_b
    tiles = jnp.transpose(products, (2, 4, 0, 1, 3, 5)).reshape(slots * enc_count, -1, tile_cols)
    scale_rows = jnp.transpose(scale_b, (2, 0, 1, 3)).reshape(slots, -1)

    dev_pairs = pair_list[0, 0]
    slot_ids = dev_pairs[:, 0]
    block_ids = dev_pairs[:, 1]
    amount = pair_count[0, 0]
    pair_total = dev_pairs.shape[0]
    chosen = jnp.take(tiles, slot_ids * enc_count + block_ids, axis=0, mode="clip")
    scales = jnp.take(scale_rows, slot_ids, axis=0, mode="clip").astype(jnp.float32)
    is_live = jnp.arange(pair_total) < amount
    result = jnp.where(
        is_live[:, None, None], scales[:, :, None] * chosen, jnp.zeros((), jnp.float32)
    ).astype(jnp.bfloat16)
    return result[None, None]


def solution(mesh):
    n_grp, n_shard = mesh.devices.shape
    n_c = 2
    n_x = 4
    devs = mesh.devices.reshape(n_grp // n_c, n_c, n_x, n_shard // n_x)
    mesh4 = Mesh(devs, ("z", "c", "x", "y"))
    return jax.shard_map(
        local,
        mesh=mesh4,
        in_specs=(
            P(GRP, SHARD, None),
            P(GRP, SHARD),
            P(GRP, SHARD, None, None, None),
            P(),
            P(GRP, SHARD, None, None),
            P(GRP, SHARD),
        ),
        out_specs=P(GRP, SHARD, None, None, None),
        check_vma=False,
    )
```

```python
import jax
import jax.numpy as jnp
from jax import lax
from jax.sharding import Mesh
from jax.sharding import PartitionSpec as P

GRP = ("z", "c")
SHARD = ("x", "y")
LANES = 128


def ring_parts(block, axis, n):
    parts = [None] * n
    parts[0] = block
    left = block
    right = block
    up = [(i, (i + 1) % n) for i in range(n)]
    down = [(i, (i - 1) % n) for i in range(n)]
    for step in range(1, n // 2 + 1):
        if 2 * step == n:
            half = block.shape[0] // 2
            got_left = lax.ppermute(left[:half], axis, up)
            got_right = lax.ppermute(right[half:], axis, down)
            parts[step] = jnp.concatenate([got_left, got_right], axis=0)
        else:
            left = lax.ppermute(left, axis, up)
            right = lax.ppermute(right, axis, down)
            parts[n - step] = left
            parts[step] = right
    return parts


def local(src_rows, src_act, encoder, dest_list, pair_list, pair_count):
    nb_g = src_rows.shape[0]
    width = src_rows.shape[2]
    n_x = lax.psum(1, "x")
    n_y = lax.psum(1, "y")
    my_group = lax.axis_index("z") * lax.psum(1, "c") + lax.axis_index("c")
    my_x = lax.axis_index("x")
    my_y = lax.axis_index("y")

    ext_width = width + LANES

    is_valid = dest_list >= 0
    from_me = is_valid & (dest_list // nb_g == my_group)
    sel = jnp.sum(jnp.where(from_me, dest_list % nb_g, 0), axis=1)
    send_act = jnp.take(src_act, sel, axis=0, mode="clip")
    act_block = jnp.zeros(send_act.shape + (LANES,), src_rows.dtype)
    act_block = act_block.at[:, :, 0].set(send_act)
    send = jnp.concatenate([jnp.take(src_rows, sel, axis=0, mode="clip"), act_block], axis=-1)
    recv = lax.all_to_all(send, GRP, 0, 0, tiled=True)

    my_list = lax.dynamic_index_in_dim(dest_list, my_group, 0, keepdims=False)
    my_valid = my_list >= 0
    source = jnp.where(my_valid, my_list // nb_g, 0)
    slot_rows = jnp.take(recv, source, axis=0, mode="clip")
    slot_rows = jnp.where(my_valid[:, None, None], slot_rows, jnp.zeros((), slot_rows.dtype))
    slots, rows_dev, _ = slot_rows.shape

    split = (ext_width * 3 // 5) // LANES * LANES
    part_a = slot_rows[..., :split]
    part_b = slot_rows[..., split:]

    weights = encoder[0, 0]
    enc_count, _, tile_cols = weights.shape
    enc_a = jnp.transpose(weights[:, :split, :], (1, 0, 2)).reshape(split, enc_count * tile_cols)
    enc_b = jnp.pad(weights[:, split:, :], ((0, 0), (0, ext_width - width), (0, 0)))
    enc_b = jnp.transpose(enc_b, (1, 0, 2)).reshape(ext_width - split, enc_count * tile_cols)

    def mm(block, enc):
        flat = block.reshape(-1, block.shape[-1])
        out = jnp.dot(flat, enc, preferred_element_type=jnp.float32)
        return out.reshape(-1, enc_count, tile_cols)

    cut = (split // 2) // LANES * LANES
    a_lo = lax.all_gather(part_a[..., :cut], SHARD, axis=0, tiled=False)
    prod_lo = lax.optimization_barrier(mm(a_lo, enc_a[:cut]))
    a_hi = lax.all_gather(part_a[..., cut:], SHARD, axis=0, tiled=False)
    prod_a = prod_lo + mm(a_hi, enc_a[cut:])
    prod_a = prod_a.reshape(n_x, n_y, slots, rows_dev, enc_count, tile_cols)

    b_y = jnp.stack(ring_parts(part_b, "y", n_y), axis=0)
    b_parts = ring_parts(b_y, "x", n_x)
    prod_b = jnp.stack([mm(blk, enc_b) for blk in b_parts], axis=0)
    prod_b = prod_b.reshape(n_x, n_y, slots, rows_dev, enc_count, tile_cols)
    prod_b = jnp.roll(jnp.roll(prod_b, my_x, axis=0), my_y, axis=1)
    scale_b = jnp.stack([blk[..., width - split] for blk in b_parts], axis=0)
    scale_b = jnp.roll(jnp.roll(scale_b, my_x, axis=0), my_y, axis=1)

    products = prod_a + prod_b
    tiles = jnp.transpose(products, (2, 4, 0, 1, 3, 5)).reshape(slots * enc_count, -1, tile_cols)
    scale_rows = jnp.transpose(scale_b, (2, 0, 1, 3)).reshape(slots, -1)

    dev_pairs = pair_list[0, 0]
    slot_ids = dev_pairs[:, 0]
    block_ids = dev_pairs[:, 1]
    amount = pair_count[0, 0]
    pair_total = dev_pairs.shape[0]
    chosen = jnp.take(tiles, slot_ids * enc_count + block_ids, axis=0, mode="clip")
    scales = jnp.take(scale_rows, slot_ids, axis=0, mode="clip").astype(jnp.float32)
    is_live = jnp.arange(pair_total) < amount
    result = jnp.where(
        is_live[:, None, None], scales[:, :, None] * chosen, jnp.zeros((), jnp.float32)
    ).astype(jnp.bfloat16)
    return result[None, None]


def solution(mesh):
    n_grp, n_shard = mesh.devices.shape
    n_c = 2
    n_x = 4
    devs = mesh.devices.reshape(n_grp // n_c, n_c, n_x, n_shard // n_x)
    mesh4 = Mesh(devs, ("z", "c", "x", "y"))
    return jax.shard_map(
        local,
        mesh=mesh4,
        in_specs=(
            P(GRP, SHARD, None),
            P(GRP, SHARD),
            P(GRP, SHARD, None, None, None),
            P(),
            P(GRP, SHARD, None, None),
            P(GRP, SHARD),
        ),
        out_specs=P(GRP, SHARD, None, None, None),
        check_vma=False,
    )
```

```python
import jax
import jax.numpy as jnp
from jax import lax
from jax.sharding import Mesh
from jax.sharding import PartitionSpec as P

GRP = ("z", "c")
SHARD = ("x", "y")
LANES = 128


def ring_parts(block, axis, n):
    parts = [None] * n
    parts[0] = block
    left = block
    right = block
    up = [(i, (i + 1) % n) for i in range(n)]
    down = [(i, (i - 1) % n) for i in range(n)]
    for step in range(1, n // 2 + 1):
        if 2 * step == n:
            half = block.shape[0] // 2
            got_left = lax.ppermute(left[:half], axis, up)
            got_right = lax.ppermute(right[half:], axis, down)
            parts[step] = jnp.concatenate([got_left, got_right], axis=0)
        else:
            left = lax.ppermute(left, axis, up)
            right = lax.ppermute(right, axis, down)
            parts[n - step] = left
            parts[step] = right
    return parts


def local(src_rows, src_act, encoder, dest_list, pair_list, pair_count):
    nb_g = src_rows.shape[0]
    width = src_rows.shape[2]
    n_x = lax.psum(1, "x")
    n_y = lax.psum(1, "y")
    my_group = lax.axis_index("z") * lax.psum(1, "c") + lax.axis_index("c")
    my_x = lax.axis_index("x")
    my_y = lax.axis_index("y")

    ext_width = width + LANES

    is_valid = dest_list >= 0
    from_me = is_valid & (dest_list // nb_g == my_group)
    sel = jnp.sum(jnp.where(from_me, dest_list % nb_g, 0), axis=1)
    send_act = jnp.take(src_act, sel, axis=0, mode="clip")
    act_block = jnp.zeros(send_act.shape + (LANES,), src_rows.dtype)
    act_block = act_block.at[:, :, 0].set(send_act)
    send = jnp.concatenate([jnp.take(src_rows, sel, axis=0, mode="clip"), act_block], axis=-1)
    recv = lax.all_to_all(send, GRP, 0, 0, tiled=True)

    my_list = lax.dynamic_index_in_dim(dest_list, my_group, 0, keepdims=False)
    my_valid = my_list >= 0
    source = jnp.where(my_valid, my_list // nb_g, 0)
    slot_rows = jnp.take(recv, source, axis=0, mode="clip")
    slot_rows = jnp.where(my_valid[:, None, None], slot_rows, jnp.zeros((), slot_rows.dtype))
    slots, rows_dev, _ = slot_rows.shape

    split = (ext_width * 3 // 5 + LANES - 1) // LANES * LANES
    part_a = slot_rows[..., :split]
    part_b = slot_rows[..., split:]

    weights = encoder[0, 0]
    enc_count, _, tile_cols = weights.shape
    enc_a = jnp.transpose(weights[:, :split, :], (1, 0, 2)).reshape(split, enc_count * tile_cols)
    enc_b = jnp.pad(weights[:, split:, :], ((0, 0), (0, ext_width - width), (0, 0)))
    enc_b = jnp.transpose(enc_b, (1, 0, 2)).reshape(ext_width - split, enc_count * tile_cols)

    def mm(block, enc):
        flat = block.reshape(-1, block.shape[-1])
        out = jnp.dot(flat, enc, preferred_element_type=jnp.float32)
        return out.reshape(-1, enc_count, tile_cols)

    a_all = lax.all_gather(part_a, SHARD, axis=0, tiled=False)
    prod_a = mm(a_all, enc_a).reshape(n_x, n_y, slots, rows_dev, enc_count, tile_cols)

    b_y = jnp.stack(ring_parts(part_b, "y", n_y), axis=0)
    b_parts = ring_parts(b_y, "x", n_x)
    prod_b = jnp.stack([mm(blk, enc_b) for blk in b_parts], axis=0)
    prod_b = prod_b.reshape(n_x, n_y, slots, rows_dev, enc_count, tile_cols)
    prod_b = jnp.roll(jnp.roll(prod_b, my_x, axis=0), my_y, axis=1)
    scale_b = jnp.stack([blk[..., width - split] for blk in b_parts], axis=0)
    scale_b = jnp.roll(jnp.roll(scale_b, my_x, axis=0), my_y, axis=1)

    products = prod_a + prod_b
    tiles = jnp.transpose(products, (2, 4, 0, 1, 3, 5)).reshape(slots * enc_count, -1, tile_cols)
    scale_rows = jnp.transpose(scale_b, (2, 0, 1, 3)).reshape(slots, -1)

    dev_pairs = pair_list[0, 0]
    slot_ids = dev_pairs[:, 0]
    block_ids = dev_pairs[:, 1]
    amount = pair_count[0, 0]
    pair_total = dev_pairs.shape[0]
    chosen = jnp.take(tiles, slot_ids * enc_count + block_ids, axis=0, mode="clip")
    scales = jnp.take(scale_rows, slot_ids, axis=0, mode="clip").astype(jnp.float32)
    is_live = jnp.arange(pair_total) < amount
    result = jnp.where(
        is_live[:, None, None], scales[:, :, None] * chosen, jnp.zeros((), jnp.float32)
    ).astype(jnp.bfloat16)
    return result[None, None]


def solution(mesh):
    n_grp, n_shard = mesh.devices.shape
    n_c = 2
    n_x = 4
    devs = mesh.devices.reshape(n_grp // n_c, n_c, n_x, n_shard // n_x)
    mesh4 = Mesh(devs, ("z", "c", "x", "y"))
    return jax.shard_map(
        local,
        mesh=mesh4,
        in_specs=(
            P(GRP, SHARD, None),
            P(GRP, SHARD),
            P(GRP, SHARD, None, None, None),
            P(),
            P(GRP, SHARD, None, None),
            P(GRP, SHARD),
        ),
        out_specs=P(GRP, SHARD, None, None, None),
        check_vma=False,
    )
```
